256 devices in a mesh: seq: 32 (over y, x, core), dp: 8 (over z).
Axes of the slice: x: 4, y: 4, z: 8, core: 2. Of those that a mesh axis runs over, the one named last changes fastest.
Arguments:
- query_rows: bfloat16 [8, 8192, 2048], P('dp', 'seq'), may hold values from -200 to 200
- key_rows: bfloat16 [8, 8192, 256], P('dp', 'seq'), may hold values from -6 to 6
- value_rows: bfloat16 [8, 8192, 256], P('dp', 'seq'), may hold values from -8 to 8
- file_lengths: int32 [8, 32], P('dp'), may hold values from 1 to 512, 8192 in all within a row
- residual: bfloat16 [8, 8192, 2048], P('dp', 'seq'), may hold values from -36 to 36
- w_out: bfloat16 [2048, 2048], P(None, 'dp'), may hold values from -0.125 to 0.125
- norm_gain: float32 [2048], replicated, may hold values from 0.25 to 1.75
- routes: int32 [8, 8192, 2], P('dp', 'seq'), may hold values from 0 to 31, all different within a row; in each aligned block of 256 rows (0 to 255, 256 to 511, ..., all dimensions but the last counted through in order) at most 24 rows name the same one
- route_gates: float32 [8, 8192, 2], P('dp', 'seq'), may hold values from 0.1 to 0.6
- w_gate: bfloat16 [32, 2048, 384], P('seq'), may hold values from -0.125 to 0.125
- w_up: bfloat16 [32, 2048, 384], P('seq'), may hold values from -0.125 to 0.125
- w_down: bfloat16 [32, 384, 2048], P('seq'), may hold values from -0.3125 to 0.3125
- cotangent: bfloat16 [8, 8192, 2048], P('dp', 'seq'), may hold values from -6 to 6
Outputs:
- layer_out: bfloat16 [8, 8192, 2048], P('dp', 'seq')
- grad_stream: bfloat16 [8, 8192, 2048], P('dp', 'seq')
- grad_gate: bfloat16 [32, 2048, 384], P('seq', 'dp')
- grad_up: bfloat16 [32, 2048, 384], P('seq', 'dp')
- grad_down: bfloat16 [32, 384, 2048], P('seq', None, 'dp')
The draws below stay inside these ranges and needn't reach their ends.
Inputs may be any that keep to these rules, and one draw needn't show every extreme that they name: `file_lengths`: each batch's 32 file lengths sum to 8192; the longest is exactly 512. `routes`: each token names 2 different experts. Among the tokens of one device no expert is named more than 24 times, and in every draw some device names some expert exactly 24 times.
All inputs are finite; a program needn't handle non-finite values.
Results may differ from the reference program's by a relative error of at most 0.022.
Values may be sent and summed in bfloat16 or wider, within the bound.
No kernel may reach another device: no remote copies, remote signals or barrier semaphores. Data moves between devices by JAX's collectives and lax.ppermute only.
A program may use at most 128 MiB of HBM per device.

```python
import math
import jax
import jax.numpy as jnp
import numpy as np
from jax import lax

D = 2048
HEADS = 16
KV = 2
HD = 128
FFW = 384
TOP = 2
TOK_DEV = 256
FILE_MAX = 512
BATCHES = 8
SEQ_LEN = 8192
EXPERTS = 32
CAP = 24
NFILES = 32
N_SEQ = 32


def paired(key):
    folded = jax.random.fold_in(key, 11)
    key_part, query_part = jax.random.split(folded, 2)
    keys_drawn = jnp.clip(jax.random.normal(key_part, (BATCHES, SEQ_LEN, KV * HD), jnp.float32), -6.0, 6.0)
    queries_drawn = jnp.clip(jax.random.normal(query_part, (BATCHES, SEQ_LEN, HEADS * HD), jnp.float32), -6.0, 6.0)
    return (keys_drawn, queries_drawn)


def draw_query_rows(key, part):
    return paired(key)[1].astype(jnp.bfloat16)


def draw_key_rows(key, part):
    return paired(key)[0].astype(jnp.bfloat16)


def draw_residual(key, part):
    folded = jax.random.fold_in(key, 23)
    core_key, row_key, column_key = jax.random.split(folded, 3)
    lowest = math.log(0.3)
    highest = math.log(3.0)
    row_scale = jnp.exp(jax.random.uniform(row_key, (BATCHES, SEQ_LEN, 1), jnp.float32, lowest, highest))
    column_scale = jnp.exp(jax.random.uniform(column_key, (1, 1, D), jnp.float32, lowest, highest))
    core = jnp.clip(jax.random.normal(core_key, (BATCHES, SEQ_LEN, D), jnp.float32), -4.0, 4.0)
    return (core * row_scale * column_scale).astype(jnp.bfloat16)


def steps_of(key, extent, pieces, least, top_value):
    def one(dim, parts):
        steps = jax.random.uniform(jax.random.fold_in(jax.random.fold_in(key, 6), dim), (parts,), jnp.float32, least / len(pieces), top_value / len(pieces))
        return jnp.repeat(jnp.exp(steps), extent[dim] // parts).reshape((-1,) + (1,) * (len(extent) - dim - 1))

    loudness = one(*pieces[0])
    for cut in pieces[1:]:
        loudness = loudness * one(*cut)
    return loudness


def split_up(amount, total, most, slope):
    weights = [(1 << 20) // math.isqrt(rank ** slope) + 1 for rank in range(2, amount + 1)]
    surplus, counts = total - most - (amount - 1), [1] * (amount - 1)
    while surplus > 0:
        free = [i for i in range(amount - 1) if counts[i] < most]
        whole, remaining = sum([weights[i] for i in free]), surplus
        for i in free:
            addition = min(most - counts[i], max(1, remaining * weights[i] // whole), surplus)
            counts[i] = counts[i] + addition
            surplus = surplus - addition
    return np.array([most] + counts)


def ragged(stream_key, amount, total, bound, lean):
    if amount == 2:
        one = jax.random.randint(stream_key, (), max(1, total - bound), min(bound, total - 1) + 1)
        return jnp.stack([one, total - one])
    tallies = jnp.asarray(split_up(amount, total, bound, lean), jnp.int32)
    twos = (amount - 1) // 2
    giver, sink = tallies[1:1 + 2 * twos:2], tallies[2:2 + 2 * twos:2]
    margin = jnp.minimum(giver - 1, bound - sink)
    passed = jax.random.randint(jax.random.fold_in(stream_key, 1), (twos,), 0, 1 << 20) % (margin + 1)
    tallies = tallies.at[1:1 + 2 * twos:2].set(giver - passed).at[2:2 + 2 * twos:2].set(sink + passed)
    return tallies[jax.random.permutation(jax.random.fold_in(stream_key, 2), amount)]


def deal_out(key, own, number, rows, count, top, reach, lean):
    ranking = jax.random.permutation(key, count)
    crowded, usual = portions_of(count, rows * top, reach, lean, True), portions_of(count, rows * top, reach, lean, False)
    places = jnp.arange(count)

    def named(sizes, offset_by):
        used = int((sizes > 0).sum())
        fixed = max(1, used // 4)
        moved = fixed + (places - fixed + offset_by * (used - fixed)) % max(1, count - fixed)
        return jnp.zeros((count,), jnp.int32).at[ranking[jnp.where(places < fixed, places, moved)]].set(jnp.asarray(sizes, jnp.int32))

    sizes = jnp.where(number % 4 == 0, named(crowded, number // 4), named(usual, number - number // 4 - 1))
    mixed = jax.random.permutation(jax.random.fold_in(own, 3), count)
    giver, taker = mixed[0:count // 2 * 2:2], mixed[1:count // 2 * 2:2]
    margin = jnp.minimum(sizes[giver] - 1, reach - sizes[taker]) // 2
    margin = jnp.where((giver == ranking[0]) | (taker == ranking[0]) | (sizes[taker] == 0), 0, jnp.maximum(margin, 0))
    moved = jax.random.randint(jax.random.fold_in(own, 4), (count // 2,), 0, 1 << 20) % (margin + 1)
    sizes = sizes.at[giver].add(-moved).at[taker].add(moved)
    labels = jnp.searchsorted(jnp.cumsum(sizes), jnp.arange(rows * top), side="right").astype(jnp.int32)
    grid = labels.reshape(top, rows).T
    grid = grid[jax.random.permutation(jax.random.fold_in(own, 1), rows)]
    offset_by = jax.random.randint(jax.random.fold_in(own, 2), (rows, 1), 0, top)
    return jnp.take_along_axis(grid, (jnp.arange(top)[None, :] + offset_by) % top, axis=1)


def portions_of(amount, total, most, slope, full):
    loads = [(1 << 20) // math.isqrt(grade ** slope) + 1 for grade in range(1, amount + 1)]
    largest = most if full else min(most, max(-(-total // amount), total * loads[0] // sum(loads)))
    least = 1 if total - largest >= amount - 1 else 0
    counts, spare = [largest] + [least] * (amount - 1), total - largest - least * (amount - 1)
    while spare > 0:
        free = [i for i in range(1, amount) if counts[i] < largest] or [i for i in range(1, amount) if counts[i] < most]
        mass, budget = sum([loads[i] for i in free]), spare
        for i in free:
            addition = min(most - counts[i], max(1, budget * loads[i] // mass), spare)
            counts[i] = counts[i] + addition
            spare = spare - addition
    return np.array(counts)


def scatter_about(stream_key, shape, scale, reach, shards=(), kind=jnp.bfloat16):
    level = steps_of(stream_key, shape, shards, -0.22, 0.18) if shards else 1.0
    entries = jax.random.normal(stream_key, shape, jnp.float32) * scale * level
    return jnp.minimum(jnp.maximum(entries, -reach), reach).astype(kind)


def setup_inputs(seed: int = 0) -> dict:
    splits = jax.random.split(jax.random.key(seed), 14)
    query_rows = draw_query_rows(jax.random.fold_in(splits[13], 71), 0)
    key_rows = draw_key_rows(jax.random.fold_in(splits[13], 71), 0)
    value_rows = scatter_about(splits[2], (BATCHES, SEQ_LEN, KV * HD), 2.0, 8.0, ((0, 8), (1, 32)))
    file_lengths = jax.vmap(lambda own: ragged(own, NFILES, SEQ_LEN, FILE_MAX, 2))(jax.random.split(splits[3], BATCHES)).reshape((BATCHES, NFILES)).astype(jnp.int32)
    residual = draw_residual(jax.random.fold_in(splits[13], 71), 0)
    w_out = scatter_about(splits[5], (HEADS * HD, D), (HEADS * HD) ** -0.5, 0.125, ((1, 8),))
    norm_gain = jnp.clip(1.0 + 0.15 * jax.random.normal(splits[6], (D,), jnp.float32), 0.25, 1.75)
    routes_keys = jax.random.split(jax.random.fold_in(splits[7], 1), BATCHES * SEQ_LEN // TOK_DEV)
    routes_turns = jax.random.permutation(jax.random.fold_in(splits[7], 3), BATCHES * SEQ_LEN // TOK_DEV)
    routes = jax.vmap(lambda own, number: deal_out(jax.random.fold_in(splits[7], 2), own, number, TOK_DEV, EXPERTS, TOP, CAP, 2))(routes_keys, routes_turns).reshape((BATCHES, SEQ_LEN, TOP))
    route_gates = jnp.clip(0.1 + 0.5 * jax.random.uniform(splits[8], (BATCHES, SEQ_LEN, TOP), jnp.float32) ** steps_of(splits[8], (BATCHES, SEQ_LEN, TOP), ((0, 8), (1, 32)), -0.2, 0.2), 0.1, 0.6)
    w_gate = scatter_about(splits[9], (EXPERTS, D, FFW), D ** -0.5, 0.125, ((0, 32),))
    w_up = scatter_about(splits[10], (EXPERTS, D, FFW), D ** -0.5, 0.125, ((0, 32),))
    w_down = scatter_about(splits[11], (EXPERTS, FFW, D), FFW ** -0.5, 0.3125, ((0, 32),))
    cotangent = scatter_about(splits[12], (BATCHES, SEQ_LEN, D), 1.0, 6.0, ((0, 8), (1, 32)))
    return dict(query_rows=query_rows, key_rows=key_rows, value_rows=value_rows, file_lengths=file_lengths, residual=residual, w_out=w_out, norm_gain=norm_gain, routes=routes, route_gates=route_gates, w_gate=w_gate, w_up=w_up, w_down=w_down, cotangent=cotangent)


epsilon = 1e-06
masked = -1e+30

def normed(stream, gain):
    inverse = lax.rsqrt(lax.optimization_barrier(jnp.mean(stream * stream, axis=-1, keepdims=True)) + epsilon)
    return stream * inverse * gain

def file_index(places, ends):
    hits = (ends[None, :] <= places[:, None]).astype(jnp.int32)
    return lax.optimization_barrier(jnp.sum(hits, axis=1)).astype(jnp.int32)

def slot_targets(chosen, experts_all, capacity):
    flat_ids = chosen.reshape(-1).astype(jnp.int32)
    onehot = (flat_ids[:, None] == jnp.arange(experts_all, dtype=jnp.int32)[None, :]).astype(jnp.int32)
    earlier = (jnp.cumsum(onehot, axis=0) - onehot).astype(jnp.int32)
    placed = lax.optimization_barrier(jnp.sum(earlier * onehot, axis=1)).astype(jnp.int32)
    return (flat_ids * capacity + placed).astype(jnp.int32)

def attend_block(queries, keys_all, values_all, query_files, key_files, query_places, key_places):
    row_count = queries.shape[0]
    groups = HEADS // KV
    grouped = queries.reshape(row_count, KV, groups, HD).astype(jnp.float32)
    keyed = keys_all.reshape(-1, KV, HD).astype(jnp.float32)
    scores = jnp.einsum('rkgd,skd->kgrs', grouped, keyed) * HD ** (-0.5)
    allowed = (query_files[:, None] == key_files[None, :]) & (key_places[None, :] <= query_places[:, None]) & (key_places[None, :] >= 0)
    scores = jnp.where(allowed, scores, masked)
    row_max = lax.optimization_barrier(jnp.max(scores, axis=-1, keepdims=True))
    raised = jnp.exp(scores - row_max)
    probs = (raised / lax.optimization_barrier(jnp.sum(raised, axis=-1, keepdims=True))).astype(jnp.bfloat16)
    mixed = jnp.einsum('kgrs,skd->rkgd', probs.astype(jnp.float32), values_all.reshape(-1, KV, HD).astype(jnp.float32))
    return mixed.reshape(row_count, HEADS * HD).astype(jnp.bfloat16)

def expert_forward(inputs, w_gate, w_up, w_down):
    wide_in = inputs.astype(jnp.float32)
    pre_gate = jnp.einsum('secd,edf->secf', wide_in, w_gate.astype(jnp.float32))
    pre_up = jnp.einsum('secd,edf->secf', wide_in, w_up.astype(jnp.float32))
    hidden = (jax.nn.silu(pre_gate) * pre_up).astype(jnp.bfloat16)
    result = jnp.einsum('secf,efd->secd', hidden.astype(jnp.float32), w_down.astype(jnp.float32)).astype(jnp.bfloat16)
    return (pre_gate, pre_up, hidden, result)

def expert_backward(inputs, grads_in, pre_gate, pre_up, hidden, w_gate, w_up, w_down):
    wide_in = inputs.astype(jnp.float32)
    wide_grad = grads_in.astype(jnp.float32)
    grad_down = jnp.einsum('secf,secd->efd', hidden.astype(jnp.float32), wide_grad)
    grad_hidden = jnp.einsum('secd,efd->secf', wide_grad, w_down.astype(jnp.float32))
    sigma = jax.nn.sigmoid(pre_gate)
    grad_pre_gate = (grad_hidden * pre_up * sigma * (1.0 + pre_gate * (1.0 - sigma))).astype(jnp.bfloat16)
    grad_pre_up = (grad_hidden * pre_gate * sigma).astype(jnp.bfloat16)
    grad_gate = jnp.einsum('secd,secf->edf', wide_in, grad_pre_gate.astype(jnp.float32))
    grad_up = jnp.einsum('secd,secf->edf', wide_in, grad_pre_up.astype(jnp.float32))
    grad_inputs = jnp.einsum('secf,edf->secd', grad_pre_gate.astype(jnp.float32), w_gate.astype(jnp.float32))
    grad_inputs = grad_inputs + jnp.einsum('secf,edf->secd', grad_pre_up.astype(jnp.float32), w_up.astype(jnp.float32))
    return (grad_gate, grad_up, grad_down, grad_inputs.astype(jnp.bfloat16))

def rounded(total):
    narrow = lax.optimization_barrier(total.astype(jnp.bfloat16))
    return narrow.astype(jnp.float32)

def reference(query_rows, key_rows, value_rows, file_lengths, residual, w_out, norm_gain, routes, route_gates, w_gate, w_up, w_down, cotangent):
    rim_zeros = jnp.zeros((FILE_MAX, KV * HD), key_rows.dtype)

    def one_batch(totals, inputs):
        query_b, key_b, value_b, length_b, residual_b, route_b, gate_b, cot_b = inputs
        ends = jnp.cumsum(length_b).astype(jnp.int32)
        key_pad = jnp.concatenate([rim_zeros, key_b], axis=0)
        value_pad = jnp.concatenate([rim_zeros, value_b], axis=0)

        def block(block_index):
            row_start = (block_index * TOK_DEV).astype(jnp.int32)
            query_block = lax.dynamic_slice_in_dim(query_b, row_start, TOK_DEV, 0)
            key_block = lax.dynamic_slice_in_dim(key_pad, row_start, TOK_DEV + FILE_MAX, 0)
            value_block = lax.dynamic_slice_in_dim(value_pad, row_start, TOK_DEV + FILE_MAX, 0)
            query_places = row_start + jnp.arange(TOK_DEV, dtype=jnp.int32)
            key_places = row_start - FILE_MAX + jnp.arange(TOK_DEV + FILE_MAX, dtype=jnp.int32)
            return attend_block(query_block, key_block, value_block, file_index(query_places, ends), file_index(key_places, ends), query_places, key_places)
        attended = lax.map(block, jnp.arange(N_SEQ, dtype=jnp.int32)).reshape(SEQ_LEN, HEADS * HD)
        projected = jnp.dot(attended, w_out, preferred_element_type=jnp.float32).astype(jnp.bfloat16)
        stream = residual_b.astype(jnp.float32) + projected.astype(jnp.float32)
        normalized = normed(stream, norm_gain).astype(jnp.bfloat16)
        targets = jax.vmap(lambda chosen: slot_targets(chosen, EXPERTS, CAP))(route_b.reshape(N_SEQ, TOK_DEV, TOP))
        token_copies = jnp.repeat(normalized.reshape(N_SEQ, TOK_DEV, D), TOP, axis=1)
        slot_grad = (gate_b[:, :, None] * cot_b.astype(jnp.float32)[:, None, :]).astype(jnp.bfloat16)
        slot_grad = slot_grad.reshape(N_SEQ, TOK_DEV * TOP, D)

        def place(target, values_in):
            return jnp.zeros((EXPERTS * CAP, D), values_in.dtype).at[target].set(values_in)
        inputs_e = jax.vmap(place)(targets, token_copies).reshape(N_SEQ, EXPERTS, CAP, D)
        grads_e = jax.vmap(place)(targets, slot_grad).reshape(N_SEQ, EXPERTS, CAP, D)
        pre_gate, pre_up, hidden, expert_out = expert_forward(inputs_e, w_gate, w_up, w_down)
        grad_gate, grad_up, grad_down, grad_inputs = expert_backward(inputs_e, grads_e, pre_gate, pre_up, hidden, w_gate, w_up, w_down)

        def pick(values_in, target):
            return values_in[target]
        outputs_back = jax.vmap(pick)(expert_out.reshape(N_SEQ, EXPERTS * CAP, D), targets).reshape(SEQ_LEN, TOP, D)
        grads_back = jax.vmap(pick)(grad_inputs.reshape(N_SEQ, EXPERTS * CAP, D), targets).reshape(SEQ_LEN, TOP, D)
        mixture = lax.optimization_barrier(jnp.sum(gate_b[:, :, None] * outputs_back.astype(jnp.float32), axis=1))
        layer_b = (stream + mixture).astype(jnp.bfloat16)
        grad_normalized = lax.optimization_barrier(jnp.sum(grads_back.astype(jnp.float32), axis=1))
        pullback = jax.vjp(lambda inner: normed(inner, norm_gain), stream)[1]
        grad_stream_b = (cot_b.astype(jnp.float32) + pullback(grad_normalized)[0]).astype(jnp.bfloat16)
        new_totals = (totals[0] + rounded(grad_gate), totals[1] + rounded(grad_up), totals[2] + rounded(grad_down))
        return (new_totals, (layer_b, grad_stream_b))
    start_totals = (jnp.zeros((EXPERTS, D, FFW), jnp.float32), jnp.zeros((EXPERTS, D, FFW), jnp.float32), jnp.zeros((EXPERTS, FFW, D), jnp.float32))
    totals, stacked = lax.scan(one_batch, start_totals, (query_rows, key_rows, value_rows, file_lengths, residual, routes, route_gates, cotangent))
    return (stacked[0], stacked[1], totals[0].astype(jnp.bfloat16), totals[1].astype(jnp.bfloat16), totals[2].astype(jnp.bfloat16))
```

```python
import jax
import jax.numpy as jnp
from jax import lax
from jax.sharding import PartitionSpec as P

HEADS = 16
KV = 2
HD = 128
TOP = 2
HOPS = 2
FILE_MAX = 512


epsilon = 1e-06
masked = -1e30


def from_behind(shard, axis, by):
    peers = lax.axis_size(axis)
    pairs = [(i, i + by) for i in range(peers) if 0 <= i + by < peers]
    return lax.ppermute(shard, axis, pairs)


def normed(stream, gain):
    inverse = lax.rsqrt(jnp.mean(stream * stream, axis=-1, keepdims=True) + epsilon)
    return stream * inverse * gain


def file_index(places, ends):
    hits = (ends[None, :] <= places[:, None]).astype(jnp.int32)
    return jnp.sum(hits, axis=1)


def slot_targets(chosen, experts_all, capacity):
    flat_ids = chosen.reshape(-1)
    onehot = (flat_ids[:, None] == jnp.arange(experts_all, dtype=jnp.int32)[None, :]).astype(
        jnp.int32
    )
    earlier = jnp.cumsum(onehot, axis=0) - onehot
    placed = jnp.sum(earlier * onehot, axis=1)
    return flat_ids * capacity + placed


def attend_block(queries, keys_all, values_all, query_files, key_files, query_places, key_places):
    row_count = queries.shape[0]
    groups = HEADS // KV
    grouped = queries.reshape(row_count, KV, groups, HD)
    scores = jnp.einsum(
        "rkgd,skd->kgrs", grouped, keys_all.reshape(-1, KV, HD), preferred_element_type=jnp.float32
    ) * HD ** (-0.5)
    allowed = (
        (query_files[:, None] == key_files[None, :])
        & (key_places[None, :] <= query_places[:, None])
        & (key_places[None, :] >= 0)
    )
    scores = jnp.where(allowed, scores, masked)
    row_max = jnp.max(scores, axis=-1, keepdims=True)
    raised = jnp.exp(scores - row_max)
    probs = (raised / jnp.sum(raised, axis=-1, keepdims=True)).astype(jnp.bfloat16)
    mixed = jnp.einsum(
        "kgrs,skd->rkgd", probs, values_all.reshape(-1, KV, HD), preferred_element_type=jnp.float32
    )
    return mixed.reshape(row_count, HEADS * HD).astype(jnp.bfloat16)


def expert_forward(inputs, w_gate, w_up, w_down):
    pre_gate = jnp.einsum("secd,edf->secf", inputs, w_gate, preferred_element_type=jnp.float32)
    pre_up = jnp.einsum("secd,edf->secf", inputs, w_up, preferred_element_type=jnp.float32)
    hidden = (jax.nn.silu(pre_gate) * pre_up).astype(jnp.bfloat16)
    result = jnp.einsum(
        "secf,efd->secd", hidden, w_down, preferred_element_type=jnp.float32
    ).astype(jnp.bfloat16)
    return (pre_gate, pre_up, hidden, result)


def expert_backward(inputs, grads_in, pre_gate, pre_up, hidden, w_gate, w_up, w_down):
    grad_down = jnp.einsum("secf,secd->efd", hidden, grads_in, preferred_element_type=jnp.float32)
    grad_hidden = jnp.einsum("secd,efd->secf", grads_in, w_down, preferred_element_type=jnp.float32)
    sigma = jax.nn.sigmoid(pre_gate)
    grad_pre_gate = (grad_hidden * pre_up * sigma * (1.0 + pre_gate * (1.0 - sigma))).astype(
        jnp.bfloat16
    )
    grad_pre_up = (grad_hidden * pre_gate * sigma).astype(jnp.bfloat16)
    grad_gate = jnp.einsum(
        "secd,secf->edf", inputs, grad_pre_gate, preferred_element_type=jnp.float32
    )
    grad_up = jnp.einsum("secd,secf->edf", inputs, grad_pre_up, preferred_element_type=jnp.float32)
    grad_inputs = jnp.einsum(
        "secf,edf->secd", grad_pre_gate, w_gate, preferred_element_type=jnp.float32
    )
    grad_inputs = grad_inputs + jnp.einsum(
        "secf,edf->secd", grad_pre_up, w_up, preferred_element_type=jnp.float32
    )
    return (grad_gate, grad_up, grad_down, grad_inputs.astype(jnp.bfloat16))


def body(
    query_rows,
    key_rows,
    value_rows,
    file_lengths,
    residual,
    w_out,
    norm_gain,
    routes,
    route_gates,
    w_gate,
    w_up,
    w_down,
    cotangent,
):
    tokens = query_rows.shape[1]
    width = residual.shape[2]
    seq_count = lax.axis_size("seq")
    owned = w_gate.shape[0]
    experts_all = owned * seq_count
    capacity = max(2, 3 * tokens * TOP // (2 * experts_all))
    slots = experts_all * capacity
    seq_index = lax.axis_index("seq")
    position = seq_index * tokens

    targets = slot_targets(routes[0], experts_all, capacity)
    route_select = (
        targets[None, :] == jnp.arange(slots, dtype=jnp.int32)[:, None]
    ).astype(jnp.bfloat16)
    token_select = route_select.reshape(slots, tokens, TOP).sum(axis=2)
    sent_shape = (seq_count, owned * capacity, width)
    owner_shape = (seq_count, owned, capacity, width)

    slot_grad = (route_gates[0][:, :, None] * cotangent[0].astype(jnp.float32)[:, None, :]).astype(
        jnp.bfloat16
    )
    grads_outgoing = (
        jnp.dot(route_select, slot_grad.reshape(tokens * TOP, width), preferred_element_type=jnp.float32)
        .astype(jnp.bfloat16)
        .reshape(sent_shape)
    )
    grads_arrived = lax.all_to_all(
        grads_outgoing, "seq", split_axis=0, concat_axis=0, tiled=True
    ).reshape(owner_shape)

    rows_in = w_out.shape[0]
    half = rows_in // 2
    core = seq_index % 2
    mine = lax.all_gather(
        lax.dynamic_slice_in_dim(w_out, core * half, half, axis=0), "dp", axis=1, tiled=True
    )

    own_keys = key_rows[0]
    own_values = value_rows[0]
    own_pair = jnp.stack([own_keys, own_values])
    key_parts = []
    value_parts = []
    for distance in range(HOPS, 0, -1):
        earlier_pair = from_behind(own_pair, "seq", distance)
        key_parts.append(earlier_pair[0])
        value_parts.append(earlier_pair[1])
    keys_all = jnp.concatenate(key_parts + [own_keys], axis=0)
    values_all = jnp.concatenate(value_parts + [own_values], axis=0)
    ends = jnp.cumsum(file_lengths[0])
    query_places = position + jnp.arange(tokens, dtype=jnp.int32)
    key_places = position - FILE_MAX + jnp.arange(tokens + FILE_MAX, dtype=jnp.int32)
    attended = attend_block(
        query_rows[0],
        keys_all,
        values_all,
        file_index(query_places, ends),
        file_index(key_places, ends),
        query_places,
        key_places,
    )
    grads_arrived, mine, attended = lax.optimization_barrier((grads_arrived, mine, attended))
    other = lax.ppermute(mine, "seq", [(i, i ^ 1) for i in range(seq_count)])
    attended_mine = lax.dynamic_slice_in_dim(attended, core * half, half, axis=1)
    attended_other = lax.dynamic_slice_in_dim(attended, (1 - core) * half, half, axis=1)
    projected = (
        jnp.dot(attended_mine, mine, preferred_element_type=jnp.float32)
        + jnp.dot(attended_other, other, preferred_element_type=jnp.float32)
    ).astype(jnp.bfloat16)
    stream = residual[0].astype(jnp.float32) + projected.astype(jnp.float32)
    normalized = normed(stream, norm_gain).astype(jnp.bfloat16)
    outgoing = (
        jnp.dot(token_select, normalized, preferred_element_type=jnp.float32)
        .astype(jnp.bfloat16)
        .reshape(sent_shape)
    )
    arrived = lax.all_to_all(outgoing, "seq", split_axis=0, concat_axis=0, tiled=True).reshape(
        owner_shape
    )
    pre_gate, pre_up, hidden, expert_out = expert_forward(arrived, w_gate, w_up, w_down)
    returned = lax.all_to_all(
        expert_out.reshape(sent_shape), "seq", split_axis=0, concat_axis=0, tiled=True
    )
    grad_gate, grad_up, grad_down, grad_inputs = expert_backward(
        arrived, grads_arrived, pre_gate, pre_up, hidden, w_gate, w_up, w_down
    )
    returned, grad_inputs = lax.optimization_barrier((returned, grad_inputs))
    grads_returned = lax.all_to_all(
        grad_inputs.reshape(sent_shape), "seq", split_axis=0, concat_axis=0, tiled=True
    )
    expert_rows = lax.dot_general(
        route_select,
        returned.reshape(slots, width),
        (((0,), (0,)), ((), ())),
        preferred_element_type=jnp.float32,
    ).reshape(tokens, TOP, width)
    mixture = jnp.sum(route_gates[0][:, :, None] * expert_rows, axis=1)
    layer_out = (stream + mixture).astype(jnp.bfloat16)
    grad_normalized = lax.dot_general(
        token_select,
        grads_returned.reshape(slots, width),
        (((0,), (0,)), ((), ())),
        preferred_element_type=jnp.float32,
    )
    pullback = jax.vjp(lambda inner: normed(inner, norm_gain), stream)[1]
    grad_stream = (cotangent[0].astype(jnp.float32) + pullback(grad_normalized)[0]).astype(
        jnp.bfloat16
    )
    gate_up = lax.psum_scatter(
        jnp.concatenate([grad_gate.astype(jnp.bfloat16), grad_up.astype(jnp.bfloat16)], axis=0),
        "dp",
        scatter_dimension=1,
        tiled=True,
    )
    down = lax.psum_scatter(grad_down.astype(jnp.bfloat16), "dp", scatter_dimension=2, tiled=True)
    return (
        layer_out[None],
        grad_stream[None],
        gate_up[:owned],
        gate_up[owned:],
        down,
    )


def solution(mesh):
    return jax.shard_map(
        body,
        mesh=mesh,
        in_specs=(
            P("dp", "seq", None),
            P("dp", "seq", None),
            P("dp", "seq", None),
            P("dp", None),
            P("dp", "seq", None),
            P(None, "dp"),
            P(),
            P("dp", "seq", None),
            P("dp", "seq", None),
            P("seq", None, None),
            P("seq", None, None),
            P("seq", None, None),
            P("dp", "seq", None),
        ),
        out_specs=(
            P("dp", "seq", None),
            P("dp", "seq", None),
            P("seq", "dp", None),
            P("seq", "dp", None),
            P("seq", None, "dp"),
        ),
        check_vma=False,
    )
```

```python
import jax
import jax.numpy as jnp
from jax import lax
from jax.sharding import PartitionSpec as P

HEADS = 16
KV = 2
HD = 128
TOP = 2
HOPS = 2
FILE_MAX = 512


epsilon = 1e-06
masked = -1e30


def from_behind(shard, axis, by):
    peers = lax.axis_size(axis)
    pairs = [(i, i + by) for i in range(peers) if 0 <= i + by < peers]
    return lax.ppermute(shard, axis, pairs)


def normed(stream, gain):
    inverse = lax.rsqrt(jnp.mean(stream * stream, axis=-1, keepdims=True) + epsilon)
    return stream * inverse * gain


def file_index(places, ends):
    hits = (ends[None, :] <= places[:, None]).astype(jnp.int32)
    return jnp.sum(hits, axis=1)


def slot_targets(chosen, experts_all, capacity):
    flat_ids = chosen.reshape(-1)
    onehot = (flat_ids[:, None] == jnp.arange(experts_all, dtype=jnp.int32)[None, :]).astype(
        jnp.int32
    )
    earlier = jnp.cumsum(onehot, axis=0) - onehot
    placed = jnp.sum(earlier * onehot, axis=1)
    return flat_ids * capacity + placed


def attend_block(queries, keys_all, values_all, query_files, key_files, query_places, key_places):
    row_count = queries.shape[0]
    groups = HEADS // KV
    grouped = queries.reshape(row_count, KV, groups, HD)
    scores = jnp.einsum(
        "rkgd,skd->kgrs", grouped, keys_all.reshape(-1, KV, HD), preferred_element_type=jnp.float32
    ) * HD ** (-0.5)
    allowed = (
        (query_files[:, None] == key_files[None, :])
        & (key_places[None, :] <= query_places[:, None])
        & (key_places[None, :] >= 0)
    )
    scores = jnp.where(allowed, scores, masked)
    row_max = jnp.max(scores, axis=-1, keepdims=True)
    raised = jnp.exp(scores - row_max)
    probs = (raised / jnp.sum(raised, axis=-1, keepdims=True)).astype(jnp.bfloat16)
    mixed = jnp.einsum(
        "kgrs,skd->rkgd", probs, values_all.reshape(-1, KV, HD), preferred_element_type=jnp.float32
    )
    return mixed.reshape(row_count, HEADS * HD).astype(jnp.bfloat16)


def expert_forward(inputs, w_gate, w_up, w_down):
    pre_gate = jnp.einsum("secd,edf->secf", inputs, w_gate, preferred_element_type=jnp.float32)
    pre_up = jnp.einsum("secd,edf->secf", inputs, w_up, preferred_element_type=jnp.float32)
    hidden = (jax.nn.silu(pre_gate) * pre_up).astype(jnp.bfloat16)
    result = jnp.einsum(
        "secf,efd->secd", hidden, w_down, preferred_element_type=jnp.float32
    ).astype(jnp.bfloat16)
    return (pre_gate, pre_up, hidden, result)


def expert_backward(inputs, grads_in, pre_gate, pre_up, hidden, w_gate, w_up, w_down):
    grad_down = jnp.einsum("secf,secd->efd", hidden, grads_in, preferred_element_type=jnp.float32)
    grad_hidden = jnp.einsum("secd,efd->secf", grads_in, w_down, preferred_element_type=jnp.float32)
    sigma = jax.nn.sigmoid(pre_gate)
    grad_pre_gate = (grad_hidden * pre_up * sigma * (1.0 + pre_gate * (1.0 - sigma))).astype(
        jnp.bfloat16
    )
    grad_pre_up = (grad_hidden * pre_gate * sigma).astype(jnp.bfloat16)
    grad_gate = jnp.einsum(
        "secd,secf->edf", inputs, grad_pre_gate, preferred_element_type=jnp.float32
    )
    grad_up = jnp.einsum("secd,secf->edf", inputs, grad_pre_up, preferred_element_type=jnp.float32)
    grad_inputs = jnp.einsum(
        "secf,edf->secd", grad_pre_gate, w_gate, preferred_element_type=jnp.float32
    )
    grad_inputs = grad_inputs + jnp.einsum(
        "secf,edf->secd", grad_pre_up, w_up, preferred_element_type=jnp.float32
    )
    return (grad_gate, grad_up, grad_down, grad_inputs.astype(jnp.bfloat16))


def body(
    query_rows,
    key_rows,
    value_rows,
    file_lengths,
    residual,
    w_out,
    norm_gain,
    routes,
    route_gates,
    w_gate,
    w_up,
    w_down,
    cotangent,
):
    tokens = query_rows.shape[1]
    width = residual.shape[2]
    seq_count = lax.axis_size("seq")
    owned = w_gate.shape[0]
    experts_all = owned * seq_count
    capacity = max(2, 3 * tokens * TOP // (2 * experts_all))
    slots = experts_all * capacity
    seq_index = lax.axis_index("seq")
    position = seq_index * tokens

    targets = slot_targets(routes[0], experts_all, capacity)
    chosen = targets.reshape(tokens, TOP)
    slot_ids = jnp.arange(slots, dtype=jnp.int32)[:, None]
    route_selects = [
        (chosen[:, r][None, :] == slot_ids).astype(jnp.bfloat16) for r in range(TOP)
    ]
    token_select = sum(route_selects[1:], route_selects[0])
    sent_shape = (seq_count, owned * capacity, width)
    owner_shape = (seq_count, owned, capacity, width)

    wide_cot = cotangent[0].astype(jnp.float32)
    grads_sum = None
    for r in range(TOP):
        slot_grad_r = (route_gates[0][:, r : r + 1] * wide_cot).astype(jnp.bfloat16)
        part = jnp.dot(route_selects[r], slot_grad_r, preferred_element_type=jnp.float32)
        grads_sum = part if grads_sum is None else grads_sum + part
    grads_outgoing = grads_sum.astype(jnp.bfloat16).reshape(sent_shape)
    grads_arrived = lax.all_to_all(
        grads_outgoing, "seq", split_axis=0, concat_axis=0, tiled=True
    ).reshape(owner_shape)

    rows_in = w_out.shape[0]
    half = rows_in // 2
    core = seq_index % 2
    mine = lax.all_gather(
        lax.dynamic_slice_in_dim(w_out, core * half, half, axis=0), "dp", axis=1, tiled=True
    )

    own_keys = key_rows[0]
    own_values = value_rows[0]
    own_pair = jnp.stack([own_keys, own_values])
    key_parts = []
    value_parts = []
    for distance in range(HOPS, 0, -1):
        earlier_pair = from_behind(own_pair, "seq", distance)
        key_parts.append(earlier_pair[0])
        value_parts.append(earlier_pair[1])
    keys_all = jnp.concatenate(key_parts + [own_keys], axis=0)
    values_all = jnp.concatenate(value_parts + [own_values], axis=0)
    ends = jnp.cumsum(file_lengths[0])
    query_places = position + jnp.arange(tokens, dtype=jnp.int32)
    key_places = position - FILE_MAX + jnp.arange(tokens + FILE_MAX, dtype=jnp.int32)
    attended = attend_block(
        query_rows[0],
        keys_all,
        values_all,
        file_index(query_places, ends),
        file_index(key_places, ends),
        query_places,
        key_places,
    )
    grads_arrived, mine, attended = lax.optimization_barrier((grads_arrived, mine, attended))
    other = lax.ppermute(mine, "seq", [(i, i ^ 1) for i in range(seq_count)])
    attended_mine = lax.dynamic_slice_in_dim(attended, core * half, half, axis=1)
    attended_other = lax.dynamic_slice_in_dim(attended, (1 - core) * half, half, axis=1)
    projected = (
        jnp.dot(attended_mine, mine, preferred_element_type=jnp.float32)
        + jnp.dot(attended_other, other, preferred_element_type=jnp.float32)
    ).astype(jnp.bfloat16)
    stream = residual[0].astype(jnp.float32) + projected.astype(jnp.float32)
    normalized = normed(stream, norm_gain).astype(jnp.bfloat16)
    outgoing = (
        jnp.dot(token_select, normalized, preferred_element_type=jnp.float32)
        .astype(jnp.bfloat16)
        .reshape(sent_shape)
    )
    arrived = lax.all_to_all(outgoing, "seq", split_axis=0, concat_axis=0, tiled=True).reshape(
        owner_shape
    )
    pre_gate, pre_up, hidden, expert_out = expert_forward(arrived, w_gate, w_up, w_down)
    expert_out, arrived, grads_arrived, pre_gate, pre_up, hidden = lax.optimization_barrier(
        (expert_out, arrived, grads_arrived, pre_gate, pre_up, hidden)
    )
    returned = lax.all_to_all(
        expert_out.reshape(sent_shape), "seq", split_axis=0, concat_axis=0, tiled=True
    )
    grad_gate, grad_up, grad_down, grad_inputs = expert_backward(
        arrived, grads_arrived, pre_gate, pre_up, hidden, w_gate, w_up, w_down
    )
    returned, grad_inputs = lax.optimization_barrier((returned, grad_inputs))
    grads_returned = lax.all_to_all(
        grad_inputs.reshape(sent_shape), "seq", split_axis=0, concat_axis=0, tiled=True
    )
    returned_rows = returned.reshape(slots, width)
    mixture = None
    for r in range(TOP):
        rows_r = lax.dot_general(
            route_selects[r],
            returned_rows,
            (((0,), (0,)), ((), ())),
            preferred_element_type=jnp.float32,
        )
        term = route_gates[0][:, r : r + 1] * rows_r
        mixture = term if mixture is None else mixture + term
    layer_out = (stream + mixture).astype(jnp.bfloat16)
    grad_normalized = lax.dot_general(
        token_select,
        grads_returned.reshape(slots, width),
        (((0,), (0,)), ((), ())),
        preferred_element_type=jnp.float32,
    )
    pullback = jax.vjp(lambda inner: normed(inner, norm_gain), stream)[1]
    grad_stream = (cotangent[0].astype(jnp.float32) + pullback(grad_normalized)[0]).astype(
        jnp.bfloat16
    )
    gate_up = lax.psum_scatter(
        jnp.concatenate([grad_gate.astype(jnp.bfloat16), grad_up.astype(jnp.bfloat16)], axis=0),
        "dp",
        scatter_dimension=1,
        tiled=True,
    )
    down = lax.psum_scatter(grad_down.astype(jnp.bfloat16), "dp", scatter_dimension=2, tiled=True)
    return (
        layer_out[None],
        grad_stream[None],
        gate_up[:owned],
        gate_up[owned:],
        down,
    )


def solution(mesh):
    return jax.shard_map(
        body,
        mesh=mesh,
        in_specs=(
            P("dp", "seq", None),
            P("dp", "seq", None),
            P("dp", "seq", None),
            P("dp", None),
            P("dp", "seq", None),
            P(None, "dp"),
            P(),
            P("dp", "seq", None),
            P("dp", "seq", None),
            P("seq", None, None),
            P("seq", None, None),
            P("seq", None, None),
            P("dp", "seq", None),
        ),
        out_specs=(
            P("dp", "seq", None),
            P("dp", "seq", None),
            P("seq", "dp", None),
            P("seq", "dp", None),
            P("seq", None, "dp"),
        ),
        check_vma=False,
    )
```

```python
import jax
import jax.numpy as jnp
from jax import lax
from jax.sharding import PartitionSpec as P

HEADS = 16
KV = 2
HD = 128
TOP = 2
HOPS = 2
FILE_MAX = 512


epsilon = 1e-06
masked = -1e30


def from_behind(shard, axis, by):
    peers = lax.axis_size(axis)
    pairs = [(i, i + by) for i in range(peers) if 0 <= i + by < peers]
    return lax.ppermute(shard, axis, pairs)


def normed(stream, gain):
    inverse = lax.rsqrt(jnp.mean(stream * stream, axis=-1, keepdims=True) + epsilon)
    return stream * inverse * gain


def file_index(places, ends):
    hits = (ends[None, :] <= places[:, None]).astype(jnp.int32)
    return jnp.sum(hits, axis=1)


def slot_targets(chosen, experts_all, capacity):
    flat_ids = chosen.reshape(-1)
    onehot = (flat_ids[:, None] == jnp.arange(experts_all, dtype=jnp.int32)[None, :]).astype(
        jnp.int32
    )
    earlier = jnp.cumsum(onehot, axis=0) - onehot
    placed = jnp.sum(earlier * onehot, axis=1)
    return flat_ids * capacity + placed


def attend_block(queries, keys_all, values_all, query_files, key_files, query_places, key_places):
    row_count = queries.shape[0]
    groups = HEADS // KV
    grouped = queries.reshape(row_count, KV, groups, HD)
    scores = jnp.einsum(
        "rkgd,skd->kgrs", grouped, keys_all.reshape(-1, KV, HD), preferred_element_type=jnp.float32
    ) * HD ** (-0.5)
    allowed = (
        (query_files[:, None] == key_files[None, :])
        & (key_places[None, :] <= query_places[:, None])
        & (key_places[None, :] >= 0)
    )
    scores = jnp.where(allowed, scores, masked)
    row_max = jnp.max(scores, axis=-1, keepdims=True)
    raised = jnp.exp(scores - row_max)
    probs = (raised / jnp.sum(raised, axis=-1, keepdims=True)).astype(jnp.bfloat16)
    mixed = jnp.einsum(
        "kgrs,skd->rkgd", probs, values_all.reshape(-1, KV, HD), preferred_element_type=jnp.float32
    )
    return mixed.reshape(row_count, HEADS * HD).astype(jnp.bfloat16)


def expert_forward(inputs, w_gate, w_up, w_down):
    pre_gate = jnp.einsum("erd,edf->erf", inputs, w_gate, preferred_element_type=jnp.float32)
    pre_up = jnp.einsum("erd,edf->erf", inputs, w_up, preferred_element_type=jnp.float32)
    hidden = (jax.nn.silu(pre_gate) * pre_up).astype(jnp.bfloat16)
    result = jnp.einsum(
        "erf,efd->erd", hidden, w_down, preferred_element_type=jnp.float32
    ).astype(jnp.bfloat16)
    return (pre_gate, pre_up, hidden, result)


def expert_backward(inputs, grads_in, pre_gate, pre_up, hidden, w_gate, w_up, w_down):
    grad_down = jnp.einsum("erf,erd->efd", hidden, grads_in, preferred_element_type=jnp.float32)
    grad_hidden = jnp.einsum("erd,efd->erf", grads_in, w_down, preferred_element_type=jnp.float32)
    sigma = jax.nn.sigmoid(pre_gate)
    grad_pre_gate = (grad_hidden * pre_up * sigma * (1.0 + pre_gate * (1.0 - sigma))).astype(
        jnp.bfloat16
    )
    grad_pre_up = (grad_hidden * pre_gate * sigma).astype(jnp.bfloat16)
    grad_gate = jnp.einsum("erd,erf->edf", inputs, grad_pre_gate, preferred_element_type=jnp.float32)
    grad_up = jnp.einsum("erd,erf->edf", inputs, grad_pre_up, preferred_element_type=jnp.float32)
    grad_inputs = jnp.einsum(
        "erf,edf->erd", grad_pre_gate, w_gate, preferred_element_type=jnp.float32
    )
    grad_inputs = grad_inputs + jnp.einsum(
        "erf,edf->erd", grad_pre_up, w_up, preferred_element_type=jnp.float32
    )
    return (grad_gate, grad_up, grad_down, grad_inputs.astype(jnp.bfloat16))


def body(
    query_rows,
    key_rows,
    value_rows,
    file_lengths,
    residual,
    w_out,
    norm_gain,
    routes,
    route_gates,
    w_gate,
    w_up,
    w_down,
    cotangent,
):
    tokens = query_rows.shape[1]
    width = residual.shape[2]
    seq_count = lax.axis_size("seq")
    owned = w_gate.shape[0]
    experts_all = owned * seq_count
    capacity = max(2, 3 * tokens * TOP // (2 * experts_all))
    slots = experts_all * capacity
    seq_index = lax.axis_index("seq")
    position = seq_index * tokens

    targets = slot_targets(routes[0], experts_all, capacity)
    chosen = targets.reshape(tokens, TOP)
    slot_ids = jnp.arange(slots, dtype=jnp.int32)[:, None]
    route_selects = [
        (chosen[:, r][None, :] == slot_ids).astype(jnp.bfloat16) for r in range(TOP)
    ]
    token_select = sum(route_selects[1:], route_selects[0])
    sent_shape = (seq_count, owned * capacity, width)
    owner_shape = (seq_count, owned, capacity, width)

    wide_cot = cotangent[0].astype(jnp.float32)
    grads_sum = None
    for r in range(TOP):
        slot_grad_r = (route_gates[0][:, r : r + 1] * wide_cot).astype(jnp.bfloat16)
        part = jnp.dot(route_selects[r], slot_grad_r, preferred_element_type=jnp.float32)
        grads_sum = part if grads_sum is None else grads_sum + part
    grads_outgoing = grads_sum.astype(jnp.bfloat16).reshape(sent_shape)
    grads_arrived = lax.all_to_all(
        grads_outgoing, "seq", split_axis=0, concat_axis=0, tiled=True
    ).reshape(owner_shape)

    rows_in = w_out.shape[0]
    half = rows_in // 2
    core = seq_index % 2
    mine = lax.all_gather(
        lax.dynamic_slice_in_dim(w_out, core * half, half, axis=0), "dp", axis=1, tiled=True
    )

    own_keys = key_rows[0]
    own_values = value_rows[0]
    own_pair = jnp.stack([own_keys, own_values])
    key_parts = []
    value_parts = []
    for distance in range(HOPS, 0, -1):
        earlier_pair = from_behind(own_pair, "seq", distance)
        key_parts.append(earlier_pair[0])
        value_parts.append(earlier_pair[1])
    keys_all = jnp.concatenate(key_parts + [own_keys], axis=0)
    values_all = jnp.concatenate(value_parts + [own_values], axis=0)
    ends = jnp.cumsum(file_lengths[0])
    query_places = position + jnp.arange(tokens, dtype=jnp.int32)
    key_places = position - FILE_MAX + jnp.arange(tokens + FILE_MAX, dtype=jnp.int32)
    attended = attend_block(
        query_rows[0],
        keys_all,
        values_all,
        file_index(query_places, ends),
        file_index(key_places, ends),
        query_places,
        key_places,
    )
    grads_arrived, mine, attended = lax.optimization_barrier((grads_arrived, mine, attended))
    other = lax.ppermute(mine, "seq", [(i, i ^ 1) for i in range(seq_count)])
    attended_mine = lax.dynamic_slice_in_dim(attended, core * half, half, axis=1)
    attended_other = lax.dynamic_slice_in_dim(attended, (1 - core) * half, half, axis=1)
    projected = (
        jnp.dot(attended_mine, mine, preferred_element_type=jnp.float32)
        + jnp.dot(attended_other, other, preferred_element_type=jnp.float32)
    ).astype(jnp.bfloat16)
    stream = residual[0].astype(jnp.float32) + projected.astype(jnp.float32)
    normalized = normed(stream, norm_gain).astype(jnp.bfloat16)
    outgoing = (
        jnp.dot(token_select, normalized, preferred_element_type=jnp.float32)
        .astype(jnp.bfloat16)
        .reshape(sent_shape)
    )
    arrived = lax.all_to_all(outgoing, "seq", split_axis=0, concat_axis=0, tiled=True).reshape(
        owner_shape
    )
    rows_shape = (owned, seq_count * capacity, width)
    arrived = arrived.transpose(1, 0, 2, 3).reshape(rows_shape)
    grads_arrived = grads_arrived.transpose(1, 0, 2, 3).reshape(rows_shape)
    pre_gate, pre_up, hidden, expert_out = expert_forward(arrived, w_gate, w_up, w_down)
    expert_out, arrived, grads_arrived, pre_gate, pre_up, hidden = lax.optimization_barrier(
        (expert_out, arrived, grads_arrived, pre_gate, pre_up, hidden)
    )
    returned = lax.all_to_all(
        expert_out.reshape(owned, seq_count, capacity, width).transpose(1, 0, 2, 3).reshape(sent_shape),
        "seq",
        split_axis=0,
        concat_axis=0,
        tiled=True,
    )
    grad_gate, grad_up, grad_down, grad_inputs = expert_backward(
        arrived, grads_arrived, pre_gate, pre_up, hidden, w_gate, w_up, w_down
    )
    returned, grad_inputs = lax.optimization_barrier((returned, grad_inputs))
    grads_returned = lax.all_to_all(
        grad_inputs.reshape(owned, seq_count, capacity, width).transpose(1, 0, 2, 3).reshape(sent_shape),
        "seq",
        split_axis=0,
        concat_axis=0,
        tiled=True,
    )
    returned_rows = returned.reshape(slots, width)
    mixture = None
    for r in range(TOP):
        rows_r = lax.dot_general(
            route_selects[r],
            returned_rows,
            (((0,), (0,)), ((), ())),
            preferred_element_type=jnp.float32,
        )
        term = route_gates[0][:, r : r + 1] * rows_r
        mixture = term if mixture is None else mixture + term
    layer_out = (stream + mixture).astype(jnp.bfloat16)
    grad_normalized = lax.dot_general(
        token_select,
        grads_returned.reshape(slots, width),
        (((0,), (0,)), ((), ())),
        preferred_element_type=jnp.float32,
    )
    pullback = jax.vjp(lambda inner: normed(inner, norm_gain), stream)[1]
    grad_stream = (cotangent[0].astype(jnp.float32) + pullback(grad_normalized)[0]).astype(
        jnp.bfloat16
    )
    gate_up = lax.psum_scatter(
        jnp.concatenate([grad_gate.astype(jnp.bfloat16), grad_up.astype(jnp.bfloat16)], axis=0),
        "dp",
        scatter_dimension=1,
        tiled=True,
    )
    down = lax.psum_scatter(grad_down.astype(jnp.bfloat16), "dp", scatter_dimension=2, tiled=True)
    return (
        layer_out[None],
        grad_stream[None],
        gate_up[:owned],
        gate_up[owned:],
        down,
    )


def solution(mesh):
    return jax.shard_map(
        body,
        mesh=mesh,
        in_specs=(
            P("dp", "seq", None),
            P("dp", "seq", None),
            P("dp", "seq", None),
            P("dp", None),
            P("dp", "seq", None),
            P(None, "dp"),
            P(),
            P("dp", "seq", None),
            P("dp", "seq", None),
            P("seq", None, None),
            P("seq", None, None),
            P("seq", None, None),
            P("dp", "seq", None),
        ),
        out_specs=(
            P("dp", "seq", None),
            P("dp", "seq", None),
            P("seq", "dp", None),
            P("seq", "dp", None),
            P("seq", None, "dp"),
        ),
        check_vma=False,
    )
```

```python
import jax
import jax.numpy as jnp
from jax import lax
from jax.sharding import PartitionSpec as P

HEADS = 16
KV = 2
HD = 128
TOP = 2
HOPS = 2
FILE_MAX = 512


epsilon = 1e-06
masked = -1e30


def from_behind(shard, axis, by):
    peers = lax.axis_size(axis)
    pairs = [(i, i + by) for i in range(peers) if 0 <= i + by < peers]
    return lax.ppermute(shard, axis, pairs)


def normed(stream, gain):
    inverse = lax.rsqrt(jnp.mean(stream * stream, axis=-1, keepdims=True) + epsilon)
    return stream * inverse * gain


def file_index(places, ends):
    hits = (ends[None, :] <= places[:, None]).astype(jnp.int32)
    return jnp.sum(hits, axis=1)


def slot_targets(chosen, experts_all, capacity):
    flat_ids = chosen.reshape(-1)
    onehot = (flat_ids[:, None] == jnp.arange(experts_all, dtype=jnp.int32)[None, :]).astype(
        jnp.int32
    )
    earlier = jnp.cumsum(onehot, axis=0) - onehot
    placed = jnp.sum(earlier * onehot, axis=1)
    return flat_ids * capacity + placed


def attend_block(queries, keys_all, values_all, query_files, key_files, query_places, key_places):
    row_count = queries.shape[0]
    groups = HEADS // KV
    grouped = queries.reshape(row_count, KV, groups, HD)
    scores = jnp.einsum(
        "rkgd,skd->kgrs", grouped, keys_all.reshape(-1, KV, HD), preferred_element_type=jnp.float32
    ) * HD ** (-0.5)
    allowed = (
        (query_files[:, None] == key_files[None, :])
        & (key_places[None, :] <= query_places[:, None])
        & (key_places[None, :] >= 0)
    )
    scores = jnp.where(allowed, scores, masked)
    row_max = jnp.max(scores, axis=-1, keepdims=True)
    raised = jnp.exp(scores - row_max)
    probs = (raised / jnp.sum(raised, axis=-1, keepdims=True)).astype(jnp.bfloat16)
    mixed = jnp.einsum(
        "kgrs,skd->rkgd", probs, values_all.reshape(-1, KV, HD), preferred_element_type=jnp.float32
    )
    return mixed.reshape(row_count, HEADS * HD).astype(jnp.bfloat16)


def expert_forward(inputs, w_gate, w_up, w_down):
    pre_gate = jnp.einsum("secd,edf->secf", inputs, w_gate, preferred_element_type=jnp.float32)
    pre_up = jnp.einsum("secd,edf->secf", inputs, w_up, preferred_element_type=jnp.float32)
    hidden = (jax.nn.silu(pre_gate) * pre_up).astype(jnp.bfloat16)
    result = jnp.einsum(
        "secf,efd->secd", hidden, w_down, preferred_element_type=jnp.float32
    ).astype(jnp.bfloat16)
    return (pre_gate, pre_up, hidden, result)


def expert_backward(inputs, grads_in, pre_gate, pre_up, hidden, w_gate, w_up, w_down):
    grad_down = jnp.einsum("secf,secd->efd", hidden, grads_in, preferred_element_type=jnp.float32)
    grad_hidden = jnp.einsum("secd,efd->secf", grads_in, w_down, preferred_element_type=jnp.float32)
    sigma = jax.nn.sigmoid(pre_gate)
    grad_pre_gate = (grad_hidden * pre_up * sigma * (1.0 + pre_gate * (1.0 - sigma))).astype(
        jnp.bfloat16
    )
    grad_pre_up = (grad_hidden * pre_gate * sigma).astype(jnp.bfloat16)
    grad_gate = jnp.einsum(
        "secd,secf->edf", inputs, grad_pre_gate, preferred_element_type=jnp.float32
    )
    grad_up = jnp.einsum("secd,secf->edf", inputs, grad_pre_up, preferred_element_type=jnp.float32)
    grad_inputs = jnp.einsum(
        "secf,edf->secd", grad_pre_gate, w_gate, preferred_element_type=jnp.float32
    )
    grad_inputs = grad_inputs + jnp.einsum(
        "secf,edf->secd", grad_pre_up, w_up, preferred_element_type=jnp.float32
    )
    return (grad_gate, grad_up, grad_down, grad_inputs.astype(jnp.bfloat16))


def body(
    query_rows,
    key_rows,
    value_rows,
    file_lengths,
    residual,
    w_out,
    norm_gain,
    routes,
    route_gates,
    w_gate,
    w_up,
    w_down,
    cotangent,
):
    tokens = query_rows.shape[1]
    width = residual.shape[2]
    seq_count = lax.axis_size("seq")
    owned = w_gate.shape[0]
    experts_all = owned * seq_count
    capacity = max(2, 3 * tokens * TOP // (2 * experts_all))
    slots = experts_all * capacity
    seq_index = lax.axis_index("seq")
    position = seq_index * tokens

    targets = slot_targets(routes[0], experts_all, capacity)
    chosen = targets.reshape(tokens, TOP)
    slot_ids = jnp.arange(slots, dtype=jnp.int32)[:, None]
    route_selects = [
        (chosen[:, r][None, :] == slot_ids).astype(jnp.bfloat16) for r in range(TOP)
    ]
    token_select = sum(route_selects[1:], route_selects[0])
    lanes = 128
    if (owned * capacity * width) % (16 * lanes) == 0:
        sent_shape = (seq_count, owned * capacity * width // lanes, lanes)
    else:
        sent_shape = (seq_count, owned * capacity, width)
    owner_shape = (seq_count, owned, capacity, width)

    wide_cot = cotangent[0].astype(jnp.float32)
    grads_sum = None
    for r in range(TOP):
        slot_grad_r = (route_gates[0][:, r : r + 1] * wide_cot).astype(jnp.bfloat16)
        part = jnp.dot(route_selects[r], slot_grad_r, preferred_element_type=jnp.float32)
        grads_sum = part if grads_sum is None else grads_sum + part
    grads_outgoing = grads_sum.astype(jnp.bfloat16).reshape(sent_shape)
    grads_arrived = lax.all_to_all(
        grads_outgoing, "seq", split_axis=0, concat_axis=0, tiled=True
    ).reshape(owner_shape)

    rows_in = w_out.shape[0]
    half = rows_in // 2
    core = seq_index % 2
    mine = lax.all_gather(
        lax.dynamic_slice_in_dim(w_out, core * half, half, axis=0), "dp", axis=1, tiled=True
    )

    own_keys = key_rows[0]
    own_values = value_rows[0]
    own_pair = jnp.stack([own_keys, own_values])
    key_parts = []
    value_parts = []
    for distance in range(HOPS, 0, -1):
        earlier_pair = from_behind(own_pair, "seq", distance)
        key_parts.append(earlier_pair[0])
        value_parts.append(earlier_pair[1])
    keys_all = jnp.concatenate(key_parts + [own_keys], axis=0)
    values_all = jnp.concatenate(value_parts + [own_values], axis=0)
    ends = jnp.cumsum(file_lengths[0])
    query_places = position + jnp.arange(tokens, dtype=jnp.int32)
    key_places = position - FILE_MAX + jnp.arange(tokens + FILE_MAX, dtype=jnp.int32)
    attended = attend_block(
        query_rows[0],
        keys_all,
        values_all,
        file_index(query_places, ends),
        file_index(key_places, ends),
        query_places,
        key_places,
    )
    grads_arrived, mine, attended = lax.optimization_barrier((grads_arrived, mine, attended))
    other = lax.ppermute(mine, "seq", [(i, i ^ 1) for i in range(seq_count)])
    attended_mine = lax.dynamic_slice_in_dim(attended, core * half, half, axis=1)
    attended_other = lax.dynamic_slice_in_dim(attended, (1 - core) * half, half, axis=1)
    projected = (
        jnp.dot(attended_mine, mine, preferred_element_type=jnp.float32)
        + jnp.dot(attended_other, other, preferred_element_type=jnp.float32)
    ).astype(jnp.bfloat16)
    stream = residual[0].astype(jnp.float32) + projected.astype(jnp.float32)
    normalized = normed(stream, norm_gain).astype(jnp.bfloat16)
    outgoing = (
        jnp.dot(token_select, normalized, preferred_element_type=jnp.float32)
        .astype(jnp.bfloat16)
        .reshape(sent_shape)
    )
    arrived = lax.all_to_all(outgoing, "seq", split_axis=0, concat_axis=0, tiled=True).reshape(
        owner_shape
    )
    pre_gate, pre_up, hidden, expert_out = expert_forward(arrived, w_gate, w_up, w_down)
    expert_out, arrived, grads_arrived, pre_gate, pre_up, hidden = lax.optimization_barrier(
        (expert_out, arrived, grads_arrived, pre_gate, pre_up, hidden)
    )
    returned = lax.all_to_all(
        expert_out.reshape(sent_shape), "seq", split_axis=0, concat_axis=0, tiled=True
    )
    grad_gate, grad_up, grad_down, grad_inputs = expert_backward(
        arrived, grads_arrived, pre_gate, pre_up, hidden, w_gate, w_up, w_down
    )
    returned, grad_inputs = lax.optimization_barrier((returned, grad_inputs))
    grads_returned = lax.all_to_all(
        grad_inputs.reshape(sent_shape), "seq", split_axis=0, concat_axis=0, tiled=True
    )
    returned_rows = returned.reshape(slots, width)
    mixture = None
    for r in range(TOP):
        rows_r = lax.dot_general(
            route_selects[r],
            returned_rows,
            (((0,), (0,)), ((), ())),
            preferred_element_type=jnp.float32,
        )
        term = route_gates[0][:, r : r + 1] * rows_r
        mixture = term if mixture is None else mixture + term
    layer_out = (stream + mixture).astype(jnp.bfloat16)
    grad_normalized = lax.dot_general(
        token_select,
        grads_returned.reshape(slots, width),
        (((0,), (0,)), ((), ())),
        preferred_element_type=jnp.float32,
    )
    pullback = jax.vjp(lambda inner: normed(inner, norm_gain), stream)[1]
    grad_stream = (cotangent[0].astype(jnp.float32) + pullback(grad_normalized)[0]).astype(
        jnp.bfloat16
    )
    gate_up = lax.psum_scatter(
        jnp.concatenate([grad_gate.astype(jnp.bfloat16), grad_up.astype(jnp.bfloat16)], axis=0),
        "dp",
        scatter_dimension=1,
        tiled=True,
    )
    down = lax.psum_scatter(grad_down.astype(jnp.bfloat16), "dp", scatter_dimension=2, tiled=True)
    return (
        layer_out[None],
        grad_stream[None],
        gate_up[:owned],
        gate_up[owned:],
        down,
    )


def solution(mesh):
    return jax.shard_map(
        body,
        mesh=mesh,
        in_specs=(
            P("dp", "seq", None),
            P("dp", "seq", None),
            P("dp", "seq", None),
            P("dp", None),
            P("dp", "seq", None),
            P(None, "dp"),
            P(),
            P("dp", "seq", None),
            P("dp", "seq", None),
            P("seq", None, None),
            P("seq", None, None),
            P("seq", None, None),
            P("dp", "seq", None),
        ),
        out_specs=(
            P("dp", "seq", None),
            P("dp", "seq", None),
            P("seq", "dp", None),
            P("seq", "dp", None),
            P("seq", None, "dp"),
        ),
        check_vma=False,
    )
```

```python
import jax
import jax.numpy as jnp
from jax import lax
from jax.sharding import PartitionSpec as P

HEADS = 16
KV = 2
HD = 128
TOP = 2
HOPS = 2
FILE_MAX = 512


epsilon = 1e-06
masked = -1e30


def from_behind(shard, axis, by):
    peers = lax.axis_size(axis)
    pairs = [(i, i + by) for i in range(peers) if 0 <= i + by < peers]
    return lax.ppermute(shard, axis, pairs)


def normed(stream, gain):
    inverse = lax.rsqrt(jnp.mean(stream * stream, axis=-1, keepdims=True) + epsilon)
    return stream * inverse * gain


def file_index(places, ends):
    hits = (ends[None, :] <= places[:, None]).astype(jnp.int32)
    return jnp.sum(hits, axis=1)


def slot_targets(chosen, experts_all, capacity):
    flat_ids = chosen.reshape(-1)
    onehot = (flat_ids[:, None] == jnp.arange(experts_all, dtype=jnp.int32)[None, :]).astype(
        jnp.int32
    )
    earlier = jnp.cumsum(onehot, axis=0) - onehot
    placed = jnp.sum(earlier * onehot, axis=1)
    return flat_ids * capacity + placed


def attend_block(queries, keys_all, values_all, query_files, key_files, query_places, key_places):
    row_count = queries.shape[0]
    groups = HEADS // KV
    grouped = queries.reshape(row_count, KV, groups, HD)
    scores = jnp.einsum(
        "rkgd,skd->kgrs", grouped, keys_all.reshape(-1, KV, HD), preferred_element_type=jnp.float32
    ) * HD ** (-0.5)
    allowed = (
        (query_files[:, None] == key_files[None, :])
        & (key_places[None, :] <= query_places[:, None])
        & (key_places[None, :] >= 0)
    )
    scores = jnp.where(allowed, scores, masked)
    row_max = jnp.max(scores, axis=-1, keepdims=True)
    raised = jnp.exp(scores - row_max)
    probs = (raised / jnp.sum(raised, axis=-1, keepdims=True)).astype(jnp.bfloat16)
    mixed = jnp.einsum(
        "kgrs,skd->rkgd", probs, values_all.reshape(-1, KV, HD), preferred_element_type=jnp.float32
    )
    return mixed.reshape(row_count, HEADS * HD).astype(jnp.bfloat16)


def expert_forward(inputs, w_gate, w_up, w_down):
    pre_gate = jnp.einsum("secd,edf->secf", inputs, w_gate, preferred_element_type=jnp.float32)
    pre_up = jnp.einsum("secd,edf->secf", inputs, w_up, preferred_element_type=jnp.float32)
    hidden = (jax.nn.silu(pre_gate) * pre_up).astype(jnp.bfloat16)
    result = jnp.einsum(
        "secf,efd->secd", hidden, w_down, preferred_element_type=jnp.float32
    ).astype(jnp.bfloat16)
    return (pre_gate, pre_up, hidden, result)


def expert_backward(inputs, grads_in, pre_gate, pre_up, hidden, w_gate, w_up, w_down):
    grad_down = jnp.einsum("secf,secd->efd", hidden, grads_in, preferred_element_type=jnp.float32)
    grad_hidden = jnp.einsum("secd,efd->secf", grads_in, w_down, preferred_element_type=jnp.float32)
    sigma = jax.nn.sigmoid(pre_gate)
    grad_pre_gate = (grad_hidden * pre_up * sigma * (1.0 + pre_gate * (1.0 - sigma))).astype(
        jnp.bfloat16
    )
    grad_pre_up = (grad_hidden * pre_gate * sigma).astype(jnp.bfloat16)
    grad_gate = jnp.einsum(
        "secd,secf->edf", inputs, grad_pre_gate, preferred_element_type=jnp.float32
    )
    grad_up = jnp.einsum("secd,secf->edf", inputs, grad_pre_up, preferred_element_type=jnp.float32)
    grad_inputs = jnp.einsum(
        "secf,edf->secd", grad_pre_gate, w_gate, preferred_element_type=jnp.float32
    )
    grad_inputs = grad_inputs + jnp.einsum(
        "secf,edf->secd", grad_pre_up, w_up, preferred_element_type=jnp.float32
    )
    return (grad_gate, grad_up, grad_down, grad_inputs.astype(jnp.bfloat16))


def body(
    query_rows,
    key_rows,
    value_rows,
    file_lengths,
    residual,
    w_out,
    norm_gain,
    routes,
    route_gates,
    w_gate,
    w_up,
    w_down,
    cotangent,
):
    tokens = query_rows.shape[1]
    width = residual.shape[2]
    seq_count = lax.axis_size("seq")
    owned = w_gate.shape[0]
    experts_all = owned * seq_count
    capacity = max(2, 3 * tokens * TOP // (2 * experts_all))
    slots = experts_all * capacity
    seq_index = lax.axis_index("seq")
    position = seq_index * tokens

    targets = slot_targets(routes[0], experts_all, capacity)
    chosen = targets.reshape(tokens, TOP)
    slot_ids = jnp.arange(slots, dtype=jnp.int32)[:, None]
    route_selects = [
        (chosen[:, r][None, :] == slot_ids).astype(jnp.bfloat16) for r in range(TOP)
    ]
    token_select = sum(route_selects[1:], route_selects[0])
    sent_shape = (seq_count, owned * capacity, width)
    owner_shape = (seq_count, owned, capacity, width)

    wide_cot = cotangent[0].astype(jnp.float32)
    grads_sum = None
    for r in range(TOP):
        slot_grad_r = (route_gates[0][:, r : r + 1] * wide_cot).astype(jnp.bfloat16)
        part = jnp.dot(route_selects[r], slot_grad_r, preferred_element_type=jnp.float32)
        grads_sum = part if grads_sum is None else grads_sum + part
    grads_outgoing = grads_sum.astype(jnp.bfloat16).reshape(sent_shape)
    grads_arrived = lax.all_to_all(
        grads_outgoing, "seq", split_axis=0, concat_axis=0, tiled=True
    ).reshape(owner_shape)

    rows_in = w_out.shape[0]
    half = rows_in // 2
    core = seq_index % 2
    mine = lax.all_gather(
        lax.dynamic_slice_in_dim(w_out, core * half, half, axis=0), "dp", axis=1, tiled=True
    )

    own_keys = key_rows[0]
    own_values = value_rows[0]
    own_pair = jnp.stack([own_keys, own_values])
    key_parts = []
    value_parts = []
    for distance in range(HOPS, 0, -1):
        earlier_pair = from_behind(own_pair, "seq", distance)
        key_parts.append(earlier_pair[0])
        value_parts.append(earlier_pair[1])
    keys_all = jnp.concatenate(key_parts + [own_keys], axis=0)
    values_all = jnp.concatenate(value_parts + [own_values], axis=0)
    ends = jnp.cumsum(file_lengths[0])
    query_places = position + jnp.arange(tokens, dtype=jnp.int32)
    key_places = position - FILE_MAX + jnp.arange(tokens + FILE_MAX, dtype=jnp.int32)
    attended = attend_block(
        query_rows[0],
        keys_all,
        values_all,
        file_index(query_places, ends),
        file_index(key_places, ends),
        query_places,
        key_places,
    )
    grads_arrived, mine, attended = lax.optimization_barrier((grads_arrived, mine, attended))
    other = lax.ppermute(mine, "seq", [(i, i ^ 1) for i in range(seq_count)])
    attended_mine = lax.dynamic_slice_in_dim(attended, core * half, half, axis=1)
    attended_other = lax.dynamic_slice_in_dim(attended, (1 - core) * half, half, axis=1)
    projected = (
        jnp.dot(attended_mine, mine, preferred_element_type=jnp.float32)
        + jnp.dot(attended_other, other, preferred_element_type=jnp.float32)
    ).astype(jnp.bfloat16)
    stream = residual[0].astype(jnp.float32) + projected.astype(jnp.float32)
    normalized = normed(stream, norm_gain).astype(jnp.bfloat16)
    outgoing = (
        jnp.dot(token_select, normalized, preferred_element_type=jnp.float32)
        .astype(jnp.bfloat16)
        .reshape(sent_shape)
    )
    arrived = lax.all_to_all(outgoing, "seq", split_axis=0, concat_axis=0, tiled=True).reshape(
        owner_shape
    )
    pre_gate, pre_up, hidden, expert_out = expert_forward(arrived, w_gate, w_up, w_down)
    grad_gate, grad_up, grad_down, grad_inputs = expert_backward(
        arrived, grads_arrived, pre_gate, pre_up, hidden, w_gate, w_up, w_down
    )
    both_back = lax.all_to_all(
        jnp.concatenate(
            [expert_out.reshape(sent_shape), grad_inputs.reshape(sent_shape)], axis=1
        ),
        "seq",
        split_axis=0,
        concat_axis=0,
        tiled=True,
    )
    returned = both_back[:, : owned * capacity]
    grads_returned = both_back[:, owned * capacity :]
    returned_rows = returned.reshape(slots, width)
    mixture = None
    for r in range(TOP):
        rows_r = lax.dot_general(
            route_selects[r],
            returned_rows,
            (((0,), (0,)), ((), ())),
            preferred_element_type=jnp.float32,
        )
        term = route_gates[0][:, r : r + 1] * rows_r
        mixture = term if mixture is None else mixture + term
    layer_out = (stream + mixture).astype(jnp.bfloat16)
    grad_normalized = lax.dot_general(
        token_select,
        grads_returned.reshape(slots, width),
        (((0,), (0,)), ((), ())),
        preferred_element_type=jnp.float32,
    )
    pullback = jax.vjp(lambda inner: normed(inner, norm_gain), stream)[1]
    grad_stream = (cotangent[0].astype(jnp.float32) + pullback(grad_normalized)[0]).astype(
        jnp.bfloat16
    )
    gate_up = lax.psum_scatter(
        jnp.concatenate([grad_gate.astype(jnp.bfloat16), grad_up.astype(jnp.bfloat16)], axis=0),
        "dp",
        scatter_dimension=1,
        tiled=True,
    )
    down = lax.psum_scatter(grad_down.astype(jnp.bfloat16), "dp", scatter_dimension=2, tiled=True)
    return (
        layer_out[None],
        grad_stream[None],
        gate_up[:owned],
        gate_up[owned:],
        down,
    )


def solution(mesh):
    return jax.shard_map(
        body,
        mesh=mesh,
        in_specs=(
            P("dp", "seq", None),
            P("dp", "seq", None),
            P("dp", "seq", None),
            P("dp", None),
            P("dp", "seq", None),
            P(None, "dp"),
            P(),
            P("dp", "seq", None),
            P("dp", "seq", None),
            P("seq", None, None),
            P("seq", None, None),
            P("seq", None, None),
            P("dp", "seq", None),
        ),
        out_specs=(
            P("dp", "seq", None),
            P("dp", "seq", None),
            P("seq", "dp", None),
            P("seq", "dp", None),
            P("seq", None, "dp"),
        ),
        check_vma=False,
    )
```

```python
import jax
import jax.numpy as jnp
from jax import lax
from jax.sharding import PartitionSpec as P

HEADS = 16
KV = 2
HD = 128
TOP = 2
HOPS = 2
FILE_MAX = 512


epsilon = 1e-06
masked = -1e30


def from_behind(shard, axis, by):
    peers = lax.axis_size(axis)
    pairs = [(i, i + by) for i in range(peers) if 0 <= i + by < peers]
    return lax.ppermute(shard, axis, pairs)


def normed(stream, gain):
    inverse = lax.rsqrt(jnp.mean(stream * stream, axis=-1, keepdims=True) + epsilon)
    return stream * inverse * gain


def file_index(places, ends):
    hits = (ends[None, :] <= places[:, None]).astype(jnp.int32)
    return jnp.sum(hits, axis=1)


def slot_targets(chosen, experts_all, capacity):
    flat_ids = chosen.reshape(-1)
    onehot = (flat_ids[:, None] == jnp.arange(experts_all, dtype=jnp.int32)[None, :]).astype(
        jnp.int32
    )
    earlier = jnp.cumsum(onehot, axis=0) - onehot
    placed = jnp.sum(earlier * onehot, axis=1)
    return flat_ids * capacity + placed


def attend_block(queries, keys_all, values_all, query_files, key_files, query_places, key_places):
    row_count = queries.shape[0]
    groups = HEADS // KV
    grouped = queries.reshape(row_count, KV, groups, HD)
    scores = jnp.einsum(
        "rkgd,skd->kgrs", grouped, keys_all.reshape(-1, KV, HD), preferred_element_type=jnp.float32
    ) * HD ** (-0.5)
    allowed = (
        (query_files[:, None] == key_files[None, :])
        & (key_places[None, :] <= query_places[:, None])
        & (key_places[None, :] >= 0)
    )
    scores = jnp.where(allowed, scores, masked)
    row_max = jnp.max(scores, axis=-1, keepdims=True)
    raised = jnp.exp(scores - row_max)
    probs = (raised / jnp.sum(raised, axis=-1, keepdims=True)).astype(jnp.bfloat16)
    mixed = jnp.einsum(
        "kgrs,skd->rkgd", probs, values_all.reshape(-1, KV, HD), preferred_element_type=jnp.float32
    )
    return mixed.reshape(row_count, HEADS * HD).astype(jnp.bfloat16)


def expert_forward(inputs, w_gate, w_up, w_down):
    pre_gate = jnp.einsum("secd,edf->secf", inputs, w_gate, preferred_element_type=jnp.float32)
    pre_up = jnp.einsum("secd,edf->secf", inputs, w_up, preferred_element_type=jnp.float32)
    hidden = (jax.nn.silu(pre_gate) * pre_up).astype(jnp.bfloat16)
    result = jnp.einsum(
        "secf,efd->secd", hidden, w_down, preferred_element_type=jnp.float32
    ).astype(jnp.bfloat16)
    return (pre_gate, pre_up, hidden, result)


def expert_backward(inputs, grads_in, pre_gate, pre_up, hidden, w_gate, w_up, w_down):
    grad_down = jnp.einsum("secf,secd->efd", hidden, grads_in, preferred_element_type=jnp.float32)
    grad_hidden = jnp.einsum("secd,efd->secf", grads_in, w_down, preferred_element_type=jnp.float32)
    sigma = jax.nn.sigmoid(pre_gate)
    grad_pre_gate = (grad_hidden * pre_up * sigma * (1.0 + pre_gate * (1.0 - sigma))).astype(
        jnp.bfloat16
    )
    grad_pre_up = (grad_hidden * pre_gate * sigma).astype(jnp.bfloat16)
    grad_gate = jnp.einsum(
        "secd,secf->edf", inputs, grad_pre_gate, preferred_element_type=jnp.float32
    )
    grad_up = jnp.einsum("secd,secf->edf", inputs, grad_pre_up, preferred_element_type=jnp.float32)
    grad_inputs = jnp.einsum(
        "secf,edf->secd", grad_pre_gate, w_gate, preferred_element_type=jnp.float32
    )
    grad_inputs = grad_inputs + jnp.einsum(
        "secf,edf->secd", grad_pre_up, w_up, preferred_element_type=jnp.float32
    )
    return (grad_gate, grad_up, grad_down, grad_inputs.astype(jnp.bfloat16))


def body(
    query_rows,
    key_rows,
    value_rows,
    file_lengths,
    residual,
    w_out,
    norm_gain,
    routes,
    route_gates,
    w_gate,
    w_up,
    w_down,
    cotangent,
):
    tokens = query_rows.shape[1]
    width = residual.shape[2]
    seq_count = lax.axis_size("seq")
    owned = w_gate.shape[0]
    experts_all = owned * seq_count
    capacity = max(2, 3 * tokens * TOP // (2 * experts_all))
    slots = experts_all * capacity
    seq_index = lax.axis_index("seq")
    position = seq_index * tokens

    targets = slot_targets(routes[0], experts_all, capacity)
    chosen = targets.reshape(tokens, TOP)
    slot_ids = jnp.arange(slots, dtype=jnp.int32)[:, None]
    route_selects = [
        (chosen[:, r][None, :] == slot_ids).astype(jnp.bfloat16) for r in range(TOP)
    ]
    token_select = sum(route_selects[1:], route_selects[0])
    sent_shape = (seq_count, owned * capacity, width)
    owner_shape = (seq_count, owned, capacity, width)

    wide_cot = cotangent[0].astype(jnp.float32)
    grads_sum = None
    for r in range(TOP):
        slot_grad_r = (route_gates[0][:, r : r + 1] * wide_cot).astype(jnp.bfloat16)
        part = jnp.dot(route_selects[r], slot_grad_r, preferred_element_type=jnp.float32)
        grads_sum = part if grads_sum is None else grads_sum + part
    grads_outgoing = grads_sum.astype(jnp.bfloat16).reshape(sent_shape)
    grads_arrived = lax.all_to_all(
        grads_outgoing, "seq", split_axis=0, concat_axis=0, tiled=True
    ).reshape(owner_shape)

    rows_in = w_out.shape[0]
    half = rows_in // 2
    core = seq_index % 2
    mine = lax.all_gather(
        lax.dynamic_slice_in_dim(w_out, core * half, half, axis=0), "dp", axis=1, tiled=True
    )

    own_keys = key_rows[0]
    own_values = value_rows[0]
    own_pair = jnp.stack([own_keys, own_values])
    key_parts = []
    value_parts = []
    for distance in range(HOPS, 0, -1):
        earlier_pair = from_behind(own_pair, "seq", distance)
        key_parts.append(earlier_pair[0])
        value_parts.append(earlier_pair[1])
    keys_all = jnp.concatenate(key_parts + [own_keys], axis=0)
    values_all = jnp.concatenate(value_parts + [own_values], axis=0)
    ends = jnp.cumsum(file_lengths[0])
    query_places = position + jnp.arange(tokens, dtype=jnp.int32)
    key_places = position - FILE_MAX + jnp.arange(tokens + FILE_MAX, dtype=jnp.int32)
    attended = attend_block(
        query_rows[0],
        keys_all,
        values_all,
        file_index(query_places, ends),
        file_index(key_places, ends),
        query_places,
        key_places,
    )
    grads_arrived, mine, attended = lax.optimization_barrier((grads_arrived, mine, attended))
    piece = half // 2
    pairs = [(i, i ^ 1) for i in range(seq_count)]
    other_first = lax.ppermute(mine[:piece], "seq", pairs)
    other_second = lax.ppermute(mine[piece:], "seq", pairs)
    attended_mine = lax.dynamic_slice_in_dim(attended, core * half, half, axis=1)
    attended_other = lax.dynamic_slice_in_dim(attended, (1 - core) * half, half, axis=1)
    projected = (
        jnp.dot(attended_mine, mine, preferred_element_type=jnp.float32)
        + jnp.dot(attended_other[:, :piece], other_first, preferred_element_type=jnp.float32)
        + jnp.dot(attended_other[:, piece:], other_second, preferred_element_type=jnp.float32)
    ).astype(jnp.bfloat16)
    stream = residual[0].astype(jnp.float32) + projected.astype(jnp.float32)
    normalized = normed(stream, norm_gain).astype(jnp.bfloat16)
    outgoing = (
        jnp.dot(token_select, normalized, preferred_element_type=jnp.float32)
        .astype(jnp.bfloat16)
        .reshape(sent_shape)
    )
    arrived = lax.all_to_all(outgoing, "seq", split_axis=0, concat_axis=0, tiled=True).reshape(
        owner_shape
    )
    pre_gate, pre_up, hidden, expert_out = expert_forward(arrived, w_gate, w_up, w_down)
    expert_out, arrived, grads_arrived, pre_gate, pre_up, hidden = lax.optimization_barrier(
        (expert_out, arrived, grads_arrived, pre_gate, pre_up, hidden)
    )
    returned = lax.all_to_all(
        expert_out.reshape(sent_shape), "seq", split_axis=0, concat_axis=0, tiled=True
    )
    grad_gate, grad_up, grad_down, grad_inputs = expert_backward(
        arrived, grads_arrived, pre_gate, pre_up, hidden, w_gate, w_up, w_down
    )
    returned, grad_inputs = lax.optimization_barrier((returned, grad_inputs))
    grads_returned = lax.all_to_all(
        grad_inputs.reshape(sent_shape), "seq", split_axis=0, concat_axis=0, tiled=True
    )
    returned_rows = returned.reshape(slots, width)
    mixture = None
    for r in range(TOP):
        rows_r = lax.dot_general(
            route_selects[r],
            returned_rows,
            (((0,), (0,)), ((), ())),
            preferred_element_type=jnp.float32,
        )
        term = route_gates[0][:, r : r + 1] * rows_r
        mixture = term if mixture is None else mixture + term
    layer_out = (stream + mixture).astype(jnp.bfloat16)
    grad_normalized = lax.dot_general(
        token_select,
        grads_returned.reshape(slots, width),
        (((0,), (0,)), ((), ())),
        preferred_element_type=jnp.float32,
    )
    pullback = jax.vjp(lambda inner: normed(inner, norm_gain), stream)[1]
    grad_stream = (cotangent[0].astype(jnp.float32) + pullback(grad_normalized)[0]).astype(
        jnp.bfloat16
    )
    gate_up = lax.psum_scatter(
        jnp.concatenate([grad_gate.astype(jnp.bfloat16), grad_up.astype(jnp.bfloat16)], axis=0),
        "dp",
        scatter_dimension=1,
        tiled=True,
    )
    down = lax.psum_scatter(grad_down.astype(jnp.bfloat16), "dp", scatter_dimension=2, tiled=True)
    return (
        layer_out[None],
        grad_stream[None],
        gate_up[:owned],
        gate_up[owned:],
        down,
    )


def solution(mesh):
    return jax.shard_map(
        body,
        mesh=mesh,
        in_specs=(
            P("dp", "seq", None),
            P("dp", "seq", None),
            P("dp", "seq", None),
            P("dp", None),
            P("dp", "seq", None),
            P(None, "dp"),
            P(),
            P("dp", "seq", None),
            P("dp", "seq", None),
            P("seq", None, None),
            P("seq", None, None),
            P("seq", None, None),
            P("dp", "seq", None),
        ),
        out_specs=(
            P("dp", "seq", None),
            P("dp", "seq", None),
            P("seq", "dp", None),
            P("seq", "dp", None),
            P("seq", None, "dp"),
        ),
        check_vma=False,
    )
```
